256 devices in a mesh: seq: 8 (over x, core), vocab: 32 (over z, y).
Axes of the slice: x: 4, y: 4, z: 8, core: 2. Of those that a mesh axis runs over, the one named last changes fastest.
Arguments:
- hidden: bfloat16 [2048, 4096], P('seq'), may hold values from -48 to 48
- head_weight: bfloat16 [4096, 65536], P('seq', 'vocab'), may hold values from -0.09375 to 0.09375
- queries: float32 [16, 65536], P(None, 'vocab'), may hold values from 0 to 1, as said below
- passage_lengths: int32 [32], replicated, may hold values from 1 to 192, 2048 in all
- pairing: int32 [32], replicated, may hold values from 0 to 15
- doc_freq: int32 [65536], P('vocab'), may hold values from 0 to 4194304
Outputs:
- grad_hidden: bfloat16 [2048, 4096], P('seq', 'vocab')
- losses: float32 [2], replicated
The draws below stay inside these ranges and needn't reach their ends.
Inputs may be any that keep to these rules, and one draw needn't show every extreme that they name: `queries`: entries are nonnegative.
All inputs are finite; a program needn't handle non-finite values.
Results may differ from the reference program's by a relative error of at most 0.0039.
Values may be sent and summed in bfloat16 or wider, within the bound.
No kernel may reach another device: no remote copies, remote signals or barrier semaphores. Data moves between devices by JAX's collectives and lax.ppermute only.
A program may use at most 128 MiB of HBM per device.

```python
import math
import jax
import jax.numpy as jnp
import numpy as np
from jax import lax

D = 4096
VOC_DEV = 2048
DOCS = 4194304
VOCAB = 65536
TOKENS = 2048
PASSAGES = 32
QUERIES = 16
MOST = 192
N_VOCAB = 32


def draw_hidden(key, part):
    first_key = jax.random.fold_in(key, 0)
    values = jnp.clip(jax.random.normal(first_key, (TOKENS, D), jnp.float32), -6.0, 6.0)
    return values.astype(jnp.bfloat16)


def draw_queries(key, part):
    column = jnp.arange(VOCAB, dtype=jnp.float32)
    rising = 1.0 + 2.0 * column / (VOCAB - 1)
    spread = jax.random.uniform(key, (QUERIES, VOCAB), jnp.float32, 0.0, 2.0)
    return 0.6 / jnp.sqrt(float(VOCAB)) * rising[None, :] * spread


def draw_doc_freq(key, part):
    entry = jnp.arange(VOCAB, dtype=jnp.int32)
    upper = 1 + DOCS // VOCAB * (VOCAB - entry)
    return jax.random.randint(key, (VOCAB,), 0, upper, dtype=jnp.int32)


def touch_ends(drawn, key, low, high):
    spot = [jax.random.randint(jax.random.fold_in(key, axis), (), 0, length) for axis, length in enumerate(drawn.shape)]
    longest = drawn.shape.index(max(drawn.shape))
    beside = spot[:longest] + [(spot[longest] + 1) % drawn.shape[longest]] + spot[longest + 1:]
    return drawn.at[tuple(spot)].set(low).at[tuple(beside)].set(high)


def shard_levels(own_key, shape, cuts, smallest, top_value):
    gain, own = 1.0, jax.random.fold_in(own_key, 6)
    for axis_at, shards_of in cuts:
        draws = jnp.exp(jax.random.uniform(jax.random.fold_in(own, axis_at), (shards_of,), jnp.float32, smallest / len(cuts), top_value / len(cuts)))
        gain = gain * jnp.repeat(draws, shape[axis_at] // shards_of).reshape([-1 if axis == axis_at else 1 for axis in range(len(shape))])
    return gain


def split_up(amount, total, limit, lean):
    portions = [(1 << 20) // math.isqrt(standing ** lean) + 1 for standing in range(2, amount + 1)]
    rest, given = total - limit - (amount - 1), [1] * (amount - 1)
    while rest > 0:
        movable = [i for i in range(amount - 1) if given[i] < limit]
        mass, budget = sum([portions[i] for i in movable]), rest
        for i in movable:
            addition = min(limit - given[i], max(1, budget * portions[i] // mass), rest)
            given[i] = given[i] + addition
            rest = rest - addition
    return np.array([limit] + given)


def ragged(rng, count, total, most, skew):
    if count == 2:
        one = jax.random.randint(rng, (), max(1, total - most), min(most, total - 1) + 1)
        return jnp.stack([one, total - one])
    sizes = jnp.asarray(split_up(count, total, most, skew), jnp.int32)
    couples = (count - 1) // 2
    source_of, sink = sizes[1:1 + 2 * couples:2], sizes[2:2 + 2 * couples:2]
    room = jnp.minimum(source_of - 1, most - sink)
    passed = jax.random.randint(jax.random.fold_in(rng, 1), (couples,), 0, 1 << 20) % (room + 1)
    sizes = sizes.at[1:1 + 2 * couples:2].set(source_of - passed).at[2:2 + 2 * couples:2].set(sink + passed)
    return sizes[jax.random.permutation(jax.random.fold_in(rng, 2), count)]


def centred(stream_key, shape, width, bound, cuts=(), kind=jnp.bfloat16):
    entries = jax.random.normal(stream_key, shape, jnp.float32) * width
    if len(cuts) > 0:
        entries = shard_levels(stream_key, shape, cuts, -0.22, 0.18) * entries
    return jnp.clip(entries, min=-bound, max=bound).astype(kind)


def setup_inputs(seed: int = 0) -> dict:
    key_of = jax.random.split(jax.random.key(seed), 7)
    hidden = draw_hidden(jax.random.fold_in(key_of[6], 71), 0)
    head_weight = centred(key_of[1], (D, VOCAB), D ** -0.5, 0.09375, ((0, 8), (1, 32)))
    queries = draw_queries(jax.random.fold_in(key_of[6], 71), 0)
    passage_lengths = ragged(key_of[3], PASSAGES, TOKENS, MOST, 2).astype(jnp.int32)
    pairing = touch_ends(jax.random.randint(key_of[4], (PASSAGES,), 0, QUERIES), jax.random.fold_in(key_of[4], 1), 0, QUERIES - 1).astype(jnp.int32)
    doc_freq = draw_doc_freq(jax.random.fold_in(key_of[6], 71), 0)
    return dict(hidden=hidden, head_weight=head_weight, queries=queries, passage_lengths=passage_lengths, pairing=pairing, doc_freq=doc_freq)


sharpness = 8.0
loss_scale = 16384.0
flops_weight = 32.0
highest = lax.Precision.HIGHEST


def passage_members(passage_lengths, position):
    finish = jnp.cumsum(passage_lengths).astype(jnp.int32)
    starts = finish - passage_lengths
    inside = (position[None, :] >= starts[:, None]) & (position[None, :] < finish[:, None])
    return inside.astype(jnp.float32)


def saturate(logits):
    lifted = 1.0 + jax.nn.relu(logits)
    squared = lifted * lifted
    fourth = squared * squared
    return lifted, squared, fourth, fourth * fourth


def reference(hidden, head_weight, queries, passage_lengths, pairing, doc_freq):
    passages = passage_lengths.shape[0]
    query_count = queries.shape[0]
    vocab_total = head_weight.shape[1]
    position = jnp.arange(hidden.shape[0], dtype=jnp.int32)
    member = passage_members(passage_lengths, position)
    counts = passage_lengths.astype(jnp.float32)
    weights_all = jnp.log(1.0 + DOCS / (1.0 + doc_freq.astype(jnp.float32)))
    blocks = jnp.arange(N_VOCAB, dtype=jnp.int32)

    def forward_block(block_index):
        begin = (block_index * VOC_DEV).astype(jnp.int32)
        columns = lax.dynamic_slice_in_dim(head_weight, begin, VOC_DEV, 1)
        logits = jnp.dot(hidden, columns, preferred_element_type=jnp.float32)
        powered = saturate(logits)[3]
        totals = jnp.dot(member, powered, precision=highest)
        pooled = (jnp.log(totals) - jnp.log(counts)[:, None]) / sharpness
        col_mean = jnp.sum(pooled, axis=0) / passages
        weights_df = lax.dynamic_slice_in_dim(weights_all, begin, VOC_DEV, 0)
        query_cols = lax.dynamic_slice_in_dim(queries, begin, VOC_DEV, 1)
        return columns, logits, totals, pooled, col_mean, weights_df, query_cols

    def forward_step(state, block_index):
        scores, flops_sum = state
        columns, logits, totals, pooled, col_mean, weights_df, query_cols = forward_block(block_index)
        scores = scores + jnp.dot(query_cols, pooled.T, precision=highest)
        flops_sum = flops_sum + jnp.sum(weights_df * col_mean * col_mean)
        return (scores, flops_sum), None

    initial = (jnp.zeros((query_count, passages), jnp.float32), jnp.zeros((), jnp.float32))
    (scores, flops_sum), unused = lax.scan(forward_step, initial, blocks)
    flops_value = flops_sum / vocab_total
    onehot = (jnp.arange(query_count, dtype=jnp.int32)[:, None] == pairing[None, :]).astype(jnp.float32)
    peak_score = jnp.max(scores, axis=0)
    shifted = jnp.exp(scores - peak_score[None, :])
    denominator = jnp.sum(shifted, axis=0)
    log_total = peak_score + jnp.log(denominator)
    contrast = jnp.mean(log_total - jnp.sum(onehot * scores, axis=0))
    dscores = (shifted / denominator[None, :] - onehot) * (loss_scale / passages)
    flops_grad = loss_scale * flops_weight * 2.0 / (vocab_total * passages)

    def backward_step(gradient, block_index):
        columns, logits, totals, pooled, col_mean, weights_df, query_cols = forward_block(block_index)
        dpooled = jnp.dot(dscores.T, query_cols, precision=highest) + flops_grad * weights_df * col_mean
        factor = dpooled / totals
        spread = jnp.dot(member.T, factor, precision=highest)
        lifted, squared, fourth, powered = saturate(logits)
        seventh = fourth * squared * lifted
        dlogits = jnp.where(logits > 0, spread * seventh, 0.0).astype(jnp.bfloat16)
        gradient = gradient + lax.dot_general(dlogits, columns, (((1,), (1,)), ((), ())), preferred_element_type=jnp.float32)
        return gradient, None

    gradient, unused = lax.scan(backward_step, jnp.zeros(hidden.shape, jnp.float32), blocks)
    losses = jnp.stack([contrast, flops_value])
    return gradient.astype(jnp.bfloat16), losses
```

```python
import jax
import jax.numpy as jnp
from jax import lax
from jax.sharding import Mesh, PartitionSpec as P

DOCS = 4194304


sharpness = 8.0
loss_scale = 16384.0
flops_weight = 32.0
highest = lax.Precision.HIGHEST

SEQ = ("sx", "sc")
VOC = ("vz", "vy")


def butterfly(x, axes_sizes):
    for ax, n in axes_sizes:
        d = 1
        while d < n:
            x = jax.tree.map(
                lambda a: a + lax.ppermute(a, ax, [(i, i ^ d) for i in range(n)]), x
            )
            d *= 2
    return x


def softmax_terms(scores, pair_rows):
    onehot = (jnp.arange(scores.shape[0], dtype=jnp.int32)[:, None] == pair_rows[None, :]).astype(
        jnp.float32
    )
    peak_score = jnp.max(scores, axis=0)
    shifted = jnp.exp(scores - peak_score[None, :])
    denominator = jnp.sum(shifted, axis=0)
    log_total = peak_score + jnp.log(denominator)
    losses_each = log_total - jnp.sum(onehot * scores, axis=0)
    return (losses_each, shifted / denominator[None, :] - onehot)


def per_device(sizes, hidden, head_weight, queries, passage_lengths, pairing, doc_freq):
    n_sx, n_sc, n_vz, n_vy = sizes
    tok_rows = hidden.shape[0]
    vocab_cols = head_weight.shape[1]
    passages = passage_lengths.shape[0]
    vocab_total = vocab_cols * n_vz * n_vy
    finish = jnp.cumsum(passage_lengths)
    starts = finish - passage_lengths
    seq_index = lax.axis_index("sx") * n_sc + lax.axis_index("sc")
    position = seq_index * tok_rows + jnp.arange(tok_rows, dtype=jnp.int32)
    member = (
        (position[None, :] >= starts[:, None]) & (position[None, :] < finish[:, None])
    ).astype(jnp.float32)
    counts = passage_lengths.astype(jnp.float32)
    weights_df = jnp.log(1.0 + DOCS / (1.0 + doc_freq.astype(jnp.float32)))
    flops_grad = loss_scale * flops_weight * 2.0 / (vocab_total * passages)
    full_head = lax.all_gather(head_weight, SEQ, axis=0, tiled=True)
    logits = jnp.dot(hidden, full_head, preferred_element_type=jnp.float32)
    lifted = 1.0 + jax.nn.relu(logits)
    squared = lifted * lifted
    fourth = squared * squared
    powered = fourth * fourth
    local_sums = jnp.dot(member, powered, precision=highest)
    totals = butterfly(local_sums, [("sc", n_sc), ("sx", n_sx)])
    pooled = (jnp.log(totals) - jnp.log(counts)[:, None]) / sharpness
    col_mean = jnp.sum(pooled, axis=0) / passages
    flops_part = jnp.sum(weights_df * col_mean * col_mean) / vocab_total
    score_part = jnp.dot(queries, pooled.T, precision=highest)
    flops_row = jnp.where(jnp.arange(passages) == 0, flops_part, 0.0)[None, :]
    summed = butterfly(
        jnp.concatenate([score_part, flops_row], axis=0), [("vy", n_vy), ("vz", n_vz)]
    )
    scores, flops_value = summed[:-1], summed[-1, 0]
    losses_each, probs = softmax_terms(scores, pairing)
    contrast = jnp.mean(losses_each)
    dscores = probs * (loss_scale / passages)
    dpooled = jnp.dot(dscores.T, queries, precision=highest) + flops_grad * weights_df * col_mean
    factor = dpooled / totals
    spread = lax.dot_general(member, factor, (((0,), (0,)), ((), ())), precision=highest)
    seventh = fourth * squared * lifted
    dlogits = jnp.where(logits > 0, spread * seventh, 0.0).astype(jnp.bfloat16)
    partial = lax.dot_general(
        full_head, dlogits, (((1,), (1,)), ((), ())), preferred_element_type=jnp.float32
    )
    grad_cols = lax.psum_scatter(
        lax.psum_scatter(partial, "vz", scatter_dimension=0, tiled=True),
        "vy",
        scatter_dimension=0,
        tiled=True,
    )
    losses = jnp.stack([contrast, flops_value])
    return (grad_cols.T.astype(jnp.bfloat16), losses)


def solution(mesh):
    n_seq, n_voc = mesh.devices.shape
    n_sc = 2
    n_vy = 4
    sizes = (n_seq // n_sc, n_sc, n_voc // n_vy, n_vy)
    mesh4 = Mesh(mesh.devices.reshape(sizes), ("sx", "sc", "vz", "vy"))
    placed = (P(SEQ, None), P(SEQ, VOC), P(None, VOC), P(), P(), P(VOC))
    return jax.shard_map(
        lambda *a: per_device(sizes, *a),
        mesh=mesh4,
        in_specs=placed,
        out_specs=(P(SEQ, VOC), P()),
        check_vma=False,
    )
```

```python
import jax
import jax.numpy as jnp
from jax import lax
from jax.sharding import Mesh, PartitionSpec as P

DOCS = 4194304


sharpness = 8.0
loss_scale = 16384.0
flops_weight = 32.0
highest = lax.Precision.HIGHEST

SEQ = ("sx", "sc")
VOC = ("vz", "vy")


def butterfly(x, axes_sizes):
    for ax, n in axes_sizes:
        d = 1
        while d < n:
            x = jax.tree.map(
                lambda a: a + lax.ppermute(a, ax, [(i, i ^ d) for i in range(n)]), x
            )
            d *= 2
    return x


def halving_scatter(x, ax, n):
    me = lax.axis_index(ax)
    d = n // 2
    while d >= 1:
        h = x.shape[0] // 2
        bit = (me // d) % 2
        keep = lax.dynamic_slice_in_dim(x, bit * h, h, 0)
        send = lax.dynamic_slice_in_dim(x, (1 - bit) * h, h, 0)
        x = keep + lax.ppermute(send, ax, [(i, i ^ d) for i in range(n)])
        d //= 2
    return x


def softmax_terms(scores, pair_rows):
    onehot = (jnp.arange(scores.shape[0], dtype=jnp.int32)[:, None] == pair_rows[None, :]).astype(
        jnp.float32
    )
    peak_score = jnp.max(scores, axis=0)
    shifted = jnp.exp(scores - peak_score[None, :])
    denominator = jnp.sum(shifted, axis=0)
    log_total = peak_score + jnp.log(denominator)
    losses_each = log_total - jnp.sum(onehot * scores, axis=0)
    return (losses_each, shifted / denominator[None, :] - onehot)


def per_device(sizes, hidden, head_weight, queries, passage_lengths, pairing, doc_freq):
    n_sx, n_sc, n_vz, n_vy = sizes
    tok_rows = hidden.shape[0]
    vocab_cols = head_weight.shape[1]
    passages = passage_lengths.shape[0]
    vocab_total = vocab_cols * n_vz * n_vy
    finish = jnp.cumsum(passage_lengths)
    starts = finish - passage_lengths
    seq_index = lax.axis_index("sx") * n_sc + lax.axis_index("sc")
    position = seq_index * tok_rows + jnp.arange(tok_rows, dtype=jnp.int32)
    member = (
        (position[None, :] >= starts[:, None]) & (position[None, :] < finish[:, None])
    ).astype(jnp.float32)
    counts = passage_lengths.astype(jnp.float32)
    weights_df = jnp.log(1.0 + DOCS / (1.0 + doc_freq.astype(jnp.float32)))
    flops_grad = loss_scale * flops_weight * 2.0 / (vocab_total * passages)
    full_head = lax.all_gather(head_weight, SEQ, axis=0, tiled=True)
    logits = jnp.dot(hidden, full_head, preferred_element_type=jnp.float32)
    lifted = 1.0 + jax.nn.relu(logits)
    squared = lifted * lifted
    fourth = squared * squared
    powered = fourth * fourth
    local_sums = jnp.dot(member, powered, precision=highest)
    totals = butterfly(local_sums, [("sc", n_sc), ("sx", n_sx)])
    pooled = (jnp.log(totals) - jnp.log(counts)[:, None]) / sharpness
    col_mean = jnp.sum(pooled, axis=0) / passages
    flops_part = jnp.sum(weights_df * col_mean * col_mean) / vocab_total
    score_part = jnp.dot(queries, pooled.T, precision=highest)
    flops_row = jnp.where(jnp.arange(passages) == 0, flops_part, 0.0)[None, :]
    summed = butterfly(
        jnp.concatenate([score_part, flops_row], axis=0), [("vy", n_vy), ("vz", n_vz)]
    )
    scores, flops_value = summed[:-1], summed[-1, 0]
    losses_each, probs = softmax_terms(scores, pairing)
    contrast = jnp.mean(losses_each)
    dscores = probs * (loss_scale / passages)
    dpooled = jnp.dot(dscores.T, queries, precision=highest) + flops_grad * weights_df * col_mean
    factor = dpooled / totals
    spread = lax.dot_general(member, factor, (((0,), (0,)), ((), ())), precision=highest)
    seventh = fourth * squared * lifted
    dlogits = jnp.where(logits > 0, spread * seventh, 0.0).astype(jnp.bfloat16)
    partial = lax.dot_general(
        full_head, dlogits, (((1,), (1,)), ((), ())), preferred_element_type=jnp.float32
    )
    grad_cols = halving_scatter(
        lax.psum_scatter(partial, "vz", scatter_dimension=0, tiled=True), "vy", n_vy
    )
    losses = jnp.stack([contrast, flops_value])
    return (grad_cols.T.astype(jnp.bfloat16), losses)


def solution(mesh):
    n_seq, n_voc = mesh.devices.shape
    n_sc = 2
    n_vy = 4
    sizes = (n_seq // n_sc, n_sc, n_voc // n_vy, n_vy)
    mesh4 = Mesh(mesh.devices.reshape(sizes), ("sx", "sc", "vz", "vy"))
    placed = (P(SEQ, None), P(SEQ, VOC), P(None, VOC), P(), P(), P(VOC))
    return jax.shard_map(
        lambda *a: per_device(sizes, *a),
        mesh=mesh4,
        in_specs=placed,
        out_specs=(P(SEQ, VOC), P()),
        check_vma=False,
    )
```

```python
import jax
import jax.numpy as jnp
from jax import lax
from jax.sharding import Mesh, PartitionSpec as P

DOCS = 4194304


sharpness = 8.0
loss_scale = 16384.0
flops_weight = 32.0
highest = lax.Precision.HIGHEST

SEQ = ("sx", "sc")
VOC = ("vz", "vy")
GROUPS = 2


def butterfly(x, axes_sizes):
    for ax, n in axes_sizes:
        d = 1
        while d < n:
            x = jax.tree.map(
                lambda a: a + lax.ppermute(a, ax, [(i, i ^ d) for i in range(n)]), x
            )
            d *= 2
    return x


def halving_scatter(x, ax, n):
    me = lax.axis_index(ax)
    d = n // 2
    while d >= 1:
        h = x.shape[0] // 2
        bit = (me // d) % 2
        keep = lax.dynamic_slice_in_dim(x, bit * h, h, 0)
        send = lax.dynamic_slice_in_dim(x, (1 - bit) * h, h, 0)
        x = keep + lax.ppermute(send, ax, [(i, i ^ d) for i in range(n)])
        d //= 2
    return x


def softmax_terms(scores, pair_rows):
    onehot = (jnp.arange(scores.shape[0], dtype=jnp.int32)[:, None] == pair_rows[None, :]).astype(
        jnp.float32
    )
    peak_score = jnp.max(scores, axis=0)
    shifted = jnp.exp(scores - peak_score[None, :])
    denominator = jnp.sum(shifted, axis=0)
    log_total = peak_score + jnp.log(denominator)
    losses_each = log_total - jnp.sum(onehot * scores, axis=0)
    return (losses_each, shifted / denominator[None, :] - onehot)


def per_device(sizes, hidden, head_weight, queries, passage_lengths, pairing, doc_freq):
    n_sx, n_sc, n_vz, n_vy = sizes
    tok_rows = hidden.shape[0]
    vocab_cols = head_weight.shape[1]
    passages = passage_lengths.shape[0]
    vocab_total = vocab_cols * n_vz * n_vy
    finish = jnp.cumsum(passage_lengths)
    starts = finish - passage_lengths
    seq_index = lax.axis_index("sx") * n_sc + lax.axis_index("sc")
    position = seq_index * tok_rows + jnp.arange(tok_rows, dtype=jnp.int32)
    member = (
        (position[None, :] >= starts[:, None]) & (position[None, :] < finish[:, None])
    ).astype(jnp.float32)
    counts = passage_lengths.astype(jnp.float32)
    weights_df = jnp.log(1.0 + DOCS / (1.0 + doc_freq.astype(jnp.float32)))
    flops_grad = loss_scale * flops_weight * 2.0 / (vocab_total * passages)
    full_head = lax.all_gather(head_weight, SEQ, axis=0, tiled=True)
    logits = jnp.dot(hidden, full_head, preferred_element_type=jnp.float32)
    lifted = 1.0 + jax.nn.relu(logits)
    squared = lifted * lifted
    fourth = squared * squared
    powered = fourth * fourth
    local_sums = jnp.dot(member, powered, precision=highest)
    totals = butterfly(local_sums, [("sc", n_sc), ("sx", n_sx)])
    pooled = (jnp.log(totals) - jnp.log(counts)[:, None]) / sharpness
    col_mean = jnp.sum(pooled, axis=0) / passages
    flops_part = jnp.sum(weights_df * col_mean * col_mean) / vocab_total
    score_part = jnp.dot(queries, pooled.T, precision=highest)
    flops_row = jnp.where(jnp.arange(passages) == 0, flops_part, 0.0)[None, :]
    summed = butterfly(
        jnp.concatenate([score_part, flops_row], axis=0), [("vy", n_vy), ("vz", n_vz)]
    )
    scores, flops_value = summed[:-1], summed[-1, 0]
    losses_each, probs = softmax_terms(scores, pairing)
    contrast = jnp.mean(losses_each)
    dscores = probs * (loss_scale / passages)
    dpooled = jnp.dot(dscores.T, queries, precision=highest) + flops_grad * weights_df * col_mean
    factor = dpooled / totals
    spread = lax.dot_general(member, factor, (((0,), (0,)), ((), ())), precision=highest)
    seventh = fourth * squared * lifted
    dlogits = jnp.where(logits > 0, spread * seventh, 0.0).astype(jnp.bfloat16)
    n_out = n_vz * n_vy
    width = full_head.shape[0] // n_out
    grouped = full_head.reshape(n_out, GROUPS, width // GROUPS, vocab_cols)
    pieces = []
    for g in range(GROUPS):
        rows = grouped[:, g].reshape(-1, vocab_cols)
        partial = lax.dot_general(
            rows, dlogits, (((1,), (1,)), ((), ())), preferred_element_type=jnp.float32
        )
        pieces.append(
            halving_scatter(
                lax.psum_scatter(partial, "vz", scatter_dimension=0, tiled=True), "vy", n_vy
            )
        )
    grad_cols = jnp.concatenate(pieces, axis=0)
    losses = jnp.stack([contrast, flops_value])
    return (grad_cols.T.astype(jnp.bfloat16), losses)


def solution(mesh):
    n_seq, n_voc = mesh.devices.shape
    n_sc = 2
    n_vy = 4
    sizes = (n_seq // n_sc, n_sc, n_voc // n_vy, n_vy)
    mesh4 = Mesh(mesh.devices.reshape(sizes), ("sx", "sc", "vz", "vy"))
    placed = (P(SEQ, None), P(SEQ, VOC), P(None, VOC), P(), P(), P(VOC))
    return jax.shard_map(
        lambda *a: per_device(sizes, *a),
        mesh=mesh4,
        in_specs=placed,
        out_specs=(P(SEQ, VOC), P()),
        check_vma=False,
    )
```

```python
import jax
import jax.numpy as jnp
from jax import lax
from jax.sharding import Mesh, PartitionSpec as P

DOCS = 4194304


sharpness = 8.0
loss_scale = 16384.0
flops_weight = 32.0
highest = lax.Precision.HIGHEST

SEQ = ("sx", "sc")
VOC = ("vz", "vy")


def butterfly(x, axes_sizes):
    for ax, n in axes_sizes:
        d = 1
        while d < n:
            x = jax.tree.map(
                lambda a: a + lax.ppermute(a, ax, [(i, i ^ d) for i in range(n)]), x
            )
            d *= 2
    return x


def halving_scatter(x, ax, n):
    me = lax.axis_index(ax)
    d = n // 2
    while d >= 1:
        h = x.shape[0] // 2
        bit = (me // d) % 2
        keep = lax.dynamic_slice_in_dim(x, bit * h, h, 0)
        send = lax.dynamic_slice_in_dim(x, (1 - bit) * h, h, 0)
        x = keep + lax.ppermute(send, ax, [(i, i ^ d) for i in range(n)])
        d //= 2
    return x


def softmax_terms(scores, pair_rows):
    onehot = (jnp.arange(scores.shape[0], dtype=jnp.int32)[:, None] == pair_rows[None, :]).astype(
        jnp.float32
    )
    peak_score = jnp.max(scores, axis=0)
    shifted = jnp.exp(scores - peak_score[None, :])
    denominator = jnp.sum(shifted, axis=0)
    log_total = peak_score + jnp.log(denominator)
    losses_each = log_total - jnp.sum(onehot * scores, axis=0)
    return (losses_each, shifted / denominator[None, :] - onehot)


def per_device(sizes, hidden, head_weight, queries, passage_lengths, pairing, doc_freq):
    n_sx, n_sc, n_vz, n_vy = sizes
    tok_rows = hidden.shape[0]
    vocab_cols = head_weight.shape[1]
    passages = passage_lengths.shape[0]
    vocab_total = vocab_cols * n_vz * n_vy
    finish = jnp.cumsum(passage_lengths)
    starts = finish - passage_lengths
    seq_index = lax.axis_index("sx") * n_sc + lax.axis_index("sc")
    position = seq_index * tok_rows + jnp.arange(tok_rows, dtype=jnp.int32)
    member = (
        (position[None, :] >= starts[:, None]) & (position[None, :] < finish[:, None])
    ).astype(jnp.float32)
    counts = passage_lengths.astype(jnp.float32)
    weights_df = jnp.log(1.0 + DOCS / (1.0 + doc_freq.astype(jnp.float32)))
    flops_grad = loss_scale * flops_weight * 2.0 / (vocab_total * passages)
    full_head = lax.all_gather(head_weight, SEQ, axis=0, tiled=True)
    logits = jnp.dot(hidden, full_head, preferred_element_type=jnp.float32)
    lifted = 1.0 + jax.nn.relu(logits)
    squared = lifted * lifted
    fourth = squared * squared
    powered = fourth * fourth
    local_sums = jnp.dot(member, powered, precision=highest)
    chip_sums = butterfly(local_sums, [("sc", n_sc)])
    core = lax.axis_index("sc")
    half_cols = vocab_cols // n_sc
    mine = butterfly(
        lax.dynamic_slice_in_dim(chip_sums, core * half_cols, half_cols, 1), [("sx", n_sx)]
    )
    theirs = lax.ppermute(mine, "sc", [(0, 1), (1, 0)])
    totals = jnp.where(
        core == 0,
        jnp.concatenate([mine, theirs], axis=1),
        jnp.concatenate([theirs, mine], axis=1),
    )
    pooled = (jnp.log(totals) - jnp.log(counts)[:, None]) / sharpness
    col_mean = jnp.sum(pooled, axis=0) / passages
    flops_part = jnp.sum(weights_df * col_mean * col_mean) / vocab_total
    score_part = jnp.dot(queries, pooled.T, precision=highest)
    flops_row = jnp.where(jnp.arange(passages) == 0, flops_part, 0.0)[None, :]
    summed = butterfly(
        jnp.concatenate([score_part, flops_row], axis=0), [("vy", n_vy), ("vz", n_vz)]
    )
    scores, flops_value = summed[:-1], summed[-1, 0]
    losses_each, probs = softmax_terms(scores, pairing)
    contrast = jnp.mean(losses_each)
    dscores = probs * (loss_scale / passages)
    dpooled = jnp.dot(dscores.T, queries, precision=highest) + flops_grad * weights_df * col_mean
    factor = dpooled / totals
    spread = lax.dot_general(member, factor, (((0,), (0,)), ((), ())), precision=highest)
    seventh = fourth * squared * lifted
    dlogits = jnp.where(logits > 0, spread * seventh, 0.0).astype(jnp.bfloat16)
    partial = lax.dot_general(
        full_head, dlogits, (((1,), (1,)), ((), ())), preferred_element_type=jnp.float32
    )
    grad_cols = halving_scatter(
        lax.psum_scatter(partial, "vz", scatter_dimension=0, tiled=True), "vy", n_vy
    )
    losses = jnp.stack([contrast, flops_value])
    return (grad_cols.T.astype(jnp.bfloat16), losses)


def solution(mesh):
    n_seq, n_voc = mesh.devices.shape
    n_sc = 2
    n_vy = 4
    sizes = (n_seq // n_sc, n_sc, n_voc // n_vy, n_vy)
    mesh4 = Mesh(mesh.devices.reshape(sizes), ("sx", "sc", "vz", "vy"))
    placed = (P(SEQ, None), P(SEQ, VOC), P(None, VOC), P(), P(), P(VOC))
    return jax.shard_map(
        lambda *a: per_device(sizes, *a),
        mesh=mesh4,
        in_specs=placed,
        out_specs=(P(SEQ, VOC), P()),
        check_vma=False,
    )
```

```python
import jax
import jax.numpy as jnp
from jax import lax
from jax.sharding import Mesh, PartitionSpec as P

DOCS = 4194304


sharpness = 8.0
loss_scale = 16384.0
flops_weight = 32.0
highest = lax.Precision.HIGHEST

SEQ = ("sx", "sc")
VOC = ("vz", "vy")
SC_ROWS = 96


def butterfly(x, axes_sizes):
    for ax, n in axes_sizes:
        d = 1
        while d < n:
            x = jax.tree.map(
                lambda a: a + lax.ppermute(a, ax, [(i, i ^ d) for i in range(n)]), x
            )
            d *= 2
    return x


def halving_scatter(x, ax, n):
    me = lax.axis_index(ax)
    d = n // 2
    while d >= 1:
        h = x.shape[0] // 2
        bit = (me // d) % 2
        keep = lax.dynamic_slice_in_dim(x, bit * h, h, 0)
        send = lax.dynamic_slice_in_dim(x, (1 - bit) * h, h, 0)
        x = keep + lax.ppermute(send, ax, [(i, i ^ d) for i in range(n)])
        d //= 2
    return x


def softmax_terms(scores, pair_rows):
    onehot = (jnp.arange(scores.shape[0], dtype=jnp.int32)[:, None] == pair_rows[None, :]).astype(
        jnp.float32
    )
    peak_score = jnp.max(scores, axis=0)
    shifted = jnp.exp(scores - peak_score[None, :])
    denominator = jnp.sum(shifted, axis=0)
    log_total = peak_score + jnp.log(denominator)
    losses_each = log_total - jnp.sum(onehot * scores, axis=0)
    return (losses_each, shifted / denominator[None, :] - onehot)


def per_device(sizes, hidden, head_weight, queries, passage_lengths, pairing, doc_freq):
    n_sx, n_sc, n_vz, n_vy = sizes
    tok_rows = hidden.shape[0]
    vocab_cols = head_weight.shape[1]
    passages = passage_lengths.shape[0]
    vocab_total = vocab_cols * n_vz * n_vy
    finish = jnp.cumsum(passage_lengths)
    starts = finish - passage_lengths
    seq_index = lax.axis_index("sx") * n_sc + lax.axis_index("sc")
    position = seq_index * tok_rows + jnp.arange(tok_rows, dtype=jnp.int32)
    member = (
        (position[None, :] >= starts[:, None]) & (position[None, :] < finish[:, None])
    ).astype(jnp.float32)
    counts = passage_lengths.astype(jnp.float32)
    weights_df = jnp.log(1.0 + DOCS / (1.0 + doc_freq.astype(jnp.float32)))
    flops_grad = loss_scale * flops_weight * 2.0 / (vocab_total * passages)
    full_head = lax.all_gather(head_weight, SEQ, axis=0, tiled=True)
    logits = jnp.dot(hidden, full_head, preferred_element_type=jnp.float32)
    lifted = 1.0 + jax.nn.relu(logits)
    squared = lifted * lifted
    fourth = squared * squared
    powered = fourth * fourth
    local_sums = jnp.dot(member, powered, precision=highest)
    chip_sums = butterfly(local_sums, [("sc", n_sc)])
    core = lax.axis_index("sc")
    half_cols = vocab_cols // n_sc
    mine = butterfly(
        lax.dynamic_slice_in_dim(chip_sums, core * half_cols, half_cols, 1), [("sx", n_sx)]
    )
    theirs = lax.ppermute(mine, "sc", [(0, 1), (1, 0)])
    totals = jnp.where(
        core == 0,
        jnp.concatenate([mine, theirs], axis=1),
        jnp.concatenate([theirs, mine], axis=1),
    )
    pooled = (jnp.log(totals) - jnp.log(counts)[:, None]) / sharpness
    col_mean = jnp.sum(pooled, axis=0) / passages
    flops_part = jnp.sum(weights_df * col_mean * col_mean) / vocab_total
    score_part = jnp.dot(queries, pooled.T, precision=highest)
    flops_row = jnp.where(jnp.arange(passages) == 0, flops_part, 0.0)[None, :]
    summed = butterfly(
        jnp.concatenate([score_part, flops_row], axis=0), [("vy", n_vy), ("vz", n_vz)]
    )
    scores, flops_value = summed[:-1], summed[-1, 0]
    losses_each, probs = softmax_terms(scores, pairing)
    contrast = jnp.mean(losses_each)
    dscores = probs * (loss_scale / passages)
    dpooled = jnp.dot(dscores.T, queries, precision=highest) + flops_grad * weights_df * col_mean
    factor = dpooled / totals
    spread = lax.dot_general(member, factor, (((0,), (0,)), ((), ())), precision=highest)
    seventh = fourth * squared * lifted
    dlogits = jnp.where(logits > 0, spread * seventh, 0.0).astype(jnp.bfloat16)
    partial = lax.dot_general(
        full_head, dlogits, (((1,), (1,)), ((), ())), preferred_element_type=jnp.float32
    )
    width = partial.shape[0] // (n_vz * n_vy)
    blocks = partial.reshape(n_vz, n_vy, width, partial.shape[1])
    native_part = blocks[:, :, :SC_ROWS].reshape(-1, partial.shape[1])
    permute_part = blocks[:, :, SC_ROWS:].transpose(1, 0, 2, 3).reshape(-1, partial.shape[1])
    side = halving_scatter(halving_scatter(permute_part, "vy", n_vy), "vz", n_vz)
    main = halving_scatter(
        lax.psum_scatter(native_part, "vz", scatter_dimension=0, tiled=True), "vy", n_vy
    )
    grad_cols = jnp.concatenate([main, side], axis=0)
    losses = jnp.stack([contrast, flops_value])
    return (grad_cols.T.astype(jnp.bfloat16), losses)


def solution(mesh):
    n_seq, n_voc = mesh.devices.shape
    n_sc = 2
    n_vy = 4
    sizes = (n_seq // n_sc, n_sc, n_voc // n_vy, n_vy)
    mesh4 = Mesh(mesh.devices.reshape(sizes), ("sx", "sc", "vz", "vy"))
    placed = (P(SEQ, None), P(SEQ, VOC), P(None, VOC), P(), P(), P(VOC))
    return jax.shard_map(
        lambda *a: per_device(sizes, *a),
        mesh=mesh4,
        in_specs=placed,
        out_specs=(P(SEQ, VOC), P()),
        check_vma=False,
    )
```

```python
import jax
import jax.numpy as jnp
from jax import lax
from jax.sharding import Mesh, PartitionSpec as P

DOCS = 4194304


sharpness = 8.0
loss_scale = 16384.0
flops_weight = 32.0
highest = lax.Precision.HIGHEST

SEQ = ("sx", "sc")
VOC = ("vz", "vy")


def rounds_of(n):
    pairs = []
    d = 1
    while 2 * d < n:
        pairs.append([(i, i ^ d) for i in range(n)])
        d *= 2
    if n > 1:
        pairs.append([(i, n - 1 - i) for i in range(n)])
    return pairs


def butterfly(x, axes_sizes):
    for ax, n in axes_sizes:
        for perm in rounds_of(n):
            x = jax.tree.map(lambda a: a + lax.ppermute(a, ax, perm), x)
    return x


def halving_scatter(x, ax, n):
    me = lax.axis_index(ax)
    d = n // 2
    while d >= 1:
        h = x.shape[0] // 2
        bit = (me // d) % 2
        keep = lax.dynamic_slice_in_dim(x, bit * h, h, 0)
        send = lax.dynamic_slice_in_dim(x, (1 - bit) * h, h, 0)
        if d == n // 2:
            perm = [(i, n - 1 - i) for i in range(n)]
        else:
            perm = [(i, i ^ d) for i in range(n)]
        x = keep + lax.ppermute(send, ax, perm)
        d //= 2
    return x


def softmax_terms(scores, pair_rows):
    onehot = (jnp.arange(scores.shape[0], dtype=jnp.int32)[:, None] == pair_rows[None, :]).astype(
        jnp.float32
    )
    peak_score = jnp.max(scores, axis=0)
    shifted = jnp.exp(scores - peak_score[None, :])
    denominator = jnp.sum(shifted, axis=0)
    log_total = peak_score + jnp.log(denominator)
    losses_each = log_total - jnp.sum(onehot * scores, axis=0)
    return (losses_each, shifted / denominator[None, :] - onehot)


def per_device(sizes, hidden, head_weight, queries, passage_lengths, pairing, doc_freq):
    n_sx, n_sc, n_vz, n_vy = sizes
    tok_rows = hidden.shape[0]
    vocab_cols = head_weight.shape[1]
    passages = passage_lengths.shape[0]
    vocab_total = vocab_cols * n_vz * n_vy
    finish = jnp.cumsum(passage_lengths)
    starts = finish - passage_lengths
    seq_index = lax.axis_index("sx") * n_sc + lax.axis_index("sc")
    position = seq_index * tok_rows + jnp.arange(tok_rows, dtype=jnp.int32)
    member = (
        (position[None, :] >= starts[:, None]) & (position[None, :] < finish[:, None])
    ).astype(jnp.float32)
    counts = passage_lengths.astype(jnp.float32)
    weights_df = jnp.log(1.0 + DOCS / (1.0 + doc_freq.astype(jnp.float32)))
    flops_grad = loss_scale * flops_weight * 2.0 / (vocab_total * passages)
    full_head = lax.all_gather(head_weight, SEQ, axis=0, tiled=True)
    logits = jnp.dot(hidden, full_head, preferred_element_type=jnp.float32)
    lifted = 1.0 + jax.nn.relu(logits)
    squared = lifted * lifted
    fourth = squared * squared
    powered = fourth * fourth
    local_sums = jnp.dot(member, powered, precision=highest)
    chip_sums = butterfly(local_sums, [("sc", n_sc)])
    core = lax.axis_index("sc")
    half_cols = vocab_cols // n_sc
    mine = butterfly(
        lax.dynamic_slice_in_dim(chip_sums, core * half_cols, half_cols, 1), [("sx", n_sx)]
    )
    theirs = lax.ppermute(mine, "sc", [(0, 1), (1, 0)])
    totals = jnp.where(
        core == 0,
        jnp.concatenate([mine, theirs], axis=1),
        jnp.concatenate([theirs, mine], axis=1),
    )
    pooled = (jnp.log(totals) - jnp.log(counts)[:, None]) / sharpness
    col_mean = jnp.sum(pooled, axis=0) / passages
    flops_part = jnp.sum(weights_df * col_mean * col_mean) / vocab_total
    score_part = jnp.dot(queries, pooled.T, precision=highest)
    flops_row = jnp.where(jnp.arange(passages) == 0, flops_part, 0.0)[None, :]
    summed = butterfly(
        jnp.concatenate([score_part, flops_row], axis=0), [("vy", n_vy), ("vz", n_vz)]
    )
    scores, flops_value = summed[:-1], summed[-1, 0]
    losses_each, probs = softmax_terms(scores, pairing)
    contrast = jnp.mean(losses_each)
    dscores = probs * (loss_scale / passages)
    dpooled = jnp.dot(dscores.T, queries, precision=highest) + flops_grad * weights_df * col_mean
    factor = dpooled / totals
    spread = lax.dot_general(member, factor, (((0,), (0,)), ((), ())), precision=highest)
    seventh = fourth * squared * lifted
    dlogits = jnp.where(logits > 0, spread * seventh, 0.0).astype(jnp.bfloat16)
    partial = lax.dot_general(
        full_head, dlogits, (((1,), (1,)), ((), ())), preferred_element_type=jnp.float32
    )
    grad_cols = halving_scatter(
        lax.psum_scatter(partial, "vz", scatter_dimension=0, tiled=True), "vy", n_vy
    )
    losses = jnp.stack([contrast, flops_value])
    return (grad_cols.T.astype(jnp.bfloat16), losses)


def solution(mesh):
    n_seq, n_voc = mesh.devices.shape
    n_sc = 2
    n_vy = 4
    sizes = (n_seq // n_sc, n_sc, n_voc // n_vy, n_vy)
    mesh4 = Mesh(mesh.devices.reshape(sizes), ("sx", "sc", "vz", "vy"))
    placed = (P(SEQ, None), P(SEQ, VOC), P(None, VOC), P(), P(), P(VOC))
    return jax.shard_map(
        lambda *a: per_device(sizes, *a),
        mesh=mesh4,
        in_specs=placed,
        out_specs=(P(SEQ, VOC), P()),
        check_vma=False,
    )
```

```python
import jax
import jax.numpy as jnp
from jax import lax
from jax.sharding import Mesh, PartitionSpec as P

DOCS = 4194304


sharpness = 8.0
loss_scale = 16384.0
flops_weight = 32.0
highest = lax.Precision.HIGHEST

SEQ = ("sx", "sc")
VOC = ("vz", "vy")


def rounds_of(n):
    pairs = []
    d = 1
    while 2 * d < n:
        pairs.append([(i, i ^ d) for i in range(n)])
        d *= 2
    if n > 1:
        pairs.append([(i, n - 1 - i) for i in range(n)])
    return pairs


def butterfly(x, axes_sizes):
    for ax, n in axes_sizes:
        for perm in rounds_of(n):
            x = jax.tree.map(lambda a: a + lax.ppermute(a, ax, perm), x)
    return x


def halving_scatter(x, ax, n):
    me = lax.axis_index(ax)
    d = n // 2
    while d >= 1:
        h = x.shape[0] // 2
        bit = (me // d) % 2
        keep = lax.dynamic_slice_in_dim(x, bit * h, h, 0)
        send = lax.dynamic_slice_in_dim(x, (1 - bit) * h, h, 0)
        if d == n // 2:
            perm = [(i, n - 1 - i) for i in range(n)]
        else:
            perm = [(i, i ^ d) for i in range(n)]
        x = keep + lax.ppermute(send, ax, perm)
        d //= 2
    return x


def two_way_butterfly(x, ax, n):
    if n != 4:
        return butterfly(x, [(ax, n)])
    xor1 = [(i, i ^ 1) for i in range(n)]
    mirror = [(i, n - 1 - i) for i in range(n)]
    half = x.shape[-1] // 2
    a, b = x[..., :half], x[..., half:]
    a = a + lax.ppermute(a, ax, xor1)
    b = b + lax.ppermute(b, ax, mirror)
    a = a + lax.ppermute(a, ax, mirror)
    b = b + lax.ppermute(b, ax, xor1)
    return jnp.concatenate([a, b], axis=-1)


def two_way_scatter(x, ax, n):
    if n != 4:
        return halving_scatter(x, ax, n)
    me = lax.axis_index(ax)
    q = x.shape[0] // n
    half = x.shape[1] // 2
    first = halving_scatter(x[:, :half], ax, n)
    b = x[:, half:]
    b = jnp.concatenate([b[0:q], b[3 * q:4 * q], b[q:2 * q], b[2 * q:3 * q]], axis=0)
    group = jnp.where((me == 0) | (me == 3), 0, 1)
    keep = lax.dynamic_slice_in_dim(b, group * 2 * q, 2 * q, 0)
    send = lax.dynamic_slice_in_dim(b, (1 - group) * 2 * q, 2 * q, 0)
    b = keep + lax.ppermute(send, ax, [(i, i ^ 1) for i in range(n)])
    pos = me // 2
    keep = lax.dynamic_slice_in_dim(b, pos * q, q, 0)
    send = lax.dynamic_slice_in_dim(b, (1 - pos) * q, q, 0)
    b = keep + lax.ppermute(send, ax, [(i, n - 1 - i) for i in range(n)])
    return jnp.concatenate([first, b], axis=1)


def softmax_terms(scores, pair_rows):
    onehot = (jnp.arange(scores.shape[0], dtype=jnp.int32)[:, None] == pair_rows[None, :]).astype(
        jnp.float32
    )
    peak_score = jnp.max(scores, axis=0)
    shifted = jnp.exp(scores - peak_score[None, :])
    denominator = jnp.sum(shifted, axis=0)
    log_total = peak_score + jnp.log(denominator)
    losses_each = log_total - jnp.sum(onehot * scores, axis=0)
    return (losses_each, shifted / denominator[None, :] - onehot)


def per_device(sizes, hidden, head_weight, queries, passage_lengths, pairing, doc_freq):
    n_sx, n_sc, n_vz, n_vy = sizes
    tok_rows = hidden.shape[0]
    vocab_cols = head_weight.shape[1]
    passages = passage_lengths.shape[0]
    vocab_total = vocab_cols * n_vz * n_vy
    finish = jnp.cumsum(passage_lengths)
    starts = finish - passage_lengths
    seq_index = lax.axis_index("sx") * n_sc + lax.axis_index("sc")
    position = seq_index * tok_rows + jnp.arange(tok_rows, dtype=jnp.int32)
    member = (
        (position[None, :] >= starts[:, None]) & (position[None, :] < finish[:, None])
    ).astype(jnp.float32)
    counts = passage_lengths.astype(jnp.float32)
    weights_df = jnp.log(1.0 + DOCS / (1.0 + doc_freq.astype(jnp.float32)))
    flops_grad = loss_scale * flops_weight * 2.0 / (vocab_total * passages)
    full_head = lax.all_gather(head_weight, SEQ, axis=0, tiled=True)
    logits = jnp.dot(hidden, full_head, preferred_element_type=jnp.float32)
    lifted = 1.0 + jax.nn.relu(logits)
    squared = lifted * lifted
    fourth = squared * squared
    powered = fourth * fourth
    local_sums = jnp.dot(member, powered, precision=highest)
    chip_sums = butterfly(local_sums, [("sc", n_sc)])
    core = lax.axis_index("sc")
    half_cols = vocab_cols // n_sc
    mine = two_way_butterfly(
        lax.dynamic_slice_in_dim(chip_sums, core * half_cols, half_cols, 1), "sx", n_sx
    )
    theirs = lax.ppermute(mine, "sc", [(0, 1), (1, 0)])
    totals = jnp.where(
        core == 0,
        jnp.concatenate([mine, theirs], axis=1),
        jnp.concatenate([theirs, mine], axis=1),
    )
    pooled = (jnp.log(totals) - jnp.log(counts)[:, None]) / sharpness
    col_mean = jnp.sum(pooled, axis=0) / passages
    flops_part = jnp.sum(weights_df * col_mean * col_mean) / vocab_total
    score_part = jnp.dot(queries, pooled.T, precision=highest)
    flops_row = jnp.where(jnp.arange(passages) == 0, flops_part, 0.0)[None, :]
    summed = butterfly(
        jnp.concatenate([score_part, flops_row], axis=0), [("vy", n_vy), ("vz", n_vz)]
    )
    scores, flops_value = summed[:-1], summed[-1, 0]
    losses_each, probs = softmax_terms(scores, pairing)
    contrast = jnp.mean(losses_each)
    dscores = probs * (loss_scale / passages)
    dpooled = jnp.dot(dscores.T, queries, precision=highest) + flops_grad * weights_df * col_mean
    factor = dpooled / totals
    spread = lax.dot_general(member, factor, (((0,), (0,)), ((), ())), precision=highest)
    seventh = fourth * squared * lifted
    dlogits = jnp.where(logits > 0, spread * seventh, 0.0).astype(jnp.bfloat16)
    partial = lax.dot_general(
        full_head, dlogits, (((1,), (1,)), ((), ())), preferred_element_type=jnp.float32
    )
    grad_cols = two_way_scatter(
        lax.psum_scatter(partial, "vz", scatter_dimension=0, tiled=True), "vy", n_vy
    )
    losses = jnp.stack([contrast, flops_value])
    return (grad_cols.T.astype(jnp.bfloat16), losses)


def solution(mesh):
    n_seq, n_voc = mesh.devices.shape
    n_sc = 2
    n_vy = 4
    sizes = (n_seq // n_sc, n_sc, n_voc // n_vy, n_vy)
    mesh4 = Mesh(mesh.devices.reshape(sizes), ("sx", "sc", "vz", "vy"))
    placed = (P(SEQ, None), P(SEQ, VOC), P(None, VOC), P(), P(), P(VOC))
    return jax.shard_map(
        lambda *a: per_device(sizes, *a),
        mesh=mesh4,
        in_specs=placed,
        out_specs=(P(SEQ, VOC), P()),
        check_vma=False,
    )
```

```python
import jax
import jax.numpy as jnp
from jax import lax
from jax.sharding import Mesh, PartitionSpec as P

DOCS = 4194304


sharpness = 8.0
loss_scale = 16384.0
flops_weight = 32.0
highest = lax.Precision.HIGHEST

SEQ = ("sx", "sc")
VOC = ("vz", "vy")


def rounds_of(n):
    if n == 8:
        second = {0: 6, 6: 0, 1: 7, 7: 1, 2: 4, 4: 2, 3: 5, 5: 3}
        return [
            [(i, i ^ 1) for i in range(n)],
            [(i, second[i]) for i in range(n)],
            [(i, i ^ 2) for i in range(n)],
        ]
    pairs = []
    d = 1
    while 2 * d < n:
        pairs.append([(i, i ^ d) for i in range(n)])
        d *= 2
    if n > 1:
        pairs.append([(i, n - 1 - i) for i in range(n)])
    return pairs


def butterfly(x, axes_sizes):
    for ax, n in axes_sizes:
        for perm in rounds_of(n):
            x = jax.tree.map(lambda a: a + lax.ppermute(a, ax, perm), x)
    return x


def halving_scatter(x, ax, n):
    me = lax.axis_index(ax)
    d = n // 2
    while d >= 1:
        h = x.shape[0] // 2
        bit = (me // d) % 2
        keep = lax.dynamic_slice_in_dim(x, bit * h, h, 0)
        send = lax.dynamic_slice_in_dim(x, (1 - bit) * h, h, 0)
        if d == n // 2:
            perm = [(i, n - 1 - i) for i in range(n)]
        else:
            perm = [(i, i ^ d) for i in range(n)]
        x = keep + lax.ppermute(send, ax, perm)
        d //= 2
    return x


def softmax_terms(scores, pair_rows):
    onehot = (jnp.arange(scores.shape[0], dtype=jnp.int32)[:, None] == pair_rows[None, :]).astype(
        jnp.float32
    )
    peak_score = jnp.max(scores, axis=0)
    shifted = jnp.exp(scores - peak_score[None, :])
    denominator = jnp.sum(shifted, axis=0)
    log_total = peak_score + jnp.log(denominator)
    losses_each = log_total - jnp.sum(onehot * scores, axis=0)
    return (losses_each, shifted / denominator[None, :] - onehot)


def per_device(sizes, hidden, head_weight, queries, passage_lengths, pairing, doc_freq):
    n_sx, n_sc, n_vz, n_vy = sizes
    tok_rows = hidden.shape[0]
    vocab_cols = head_weight.shape[1]
    passages = passage_lengths.shape[0]
    vocab_total = vocab_cols * n_vz * n_vy
    finish = jnp.cumsum(passage_lengths)
    starts = finish - passage_lengths
    seq_index = lax.axis_index("sx") * n_sc + lax.axis_index("sc")
    position = seq_index * tok_rows + jnp.arange(tok_rows, dtype=jnp.int32)
    member = (
        (position[None, :] >= starts[:, None]) & (position[None, :] < finish[:, None])
    ).astype(jnp.float32)
    counts = passage_lengths.astype(jnp.float32)
    weights_df = jnp.log(1.0 + DOCS / (1.0 + doc_freq.astype(jnp.float32)))
    flops_grad = loss_scale * flops_weight * 2.0 / (vocab_total * passages)
    full_head = lax.all_gather(head_weight, SEQ, axis=0, tiled=True)
    logits = jnp.dot(hidden, full_head, preferred_element_type=jnp.float32)
    lifted = 1.0 + jax.nn.relu(logits)
    squared = lifted * lifted
    fourth = squared * squared
    powered = fourth * fourth
    local_sums = jnp.dot(member, powered, precision=highest)
    core = lax.axis_index("sc")
    half_cols = vocab_cols // n_sc
    own_half = lax.dynamic_slice_in_dim(local_sums, core * half_cols, half_cols, 1)
    other_half = lax.dynamic_slice_in_dim(local_sums, (1 - core) * half_cols, half_cols, 1)
    chip_half = own_half + lax.ppermute(other_half, "sc", [(0, 1), (1, 0)])
    mine = butterfly(chip_half, [("sx", n_sx)])
    theirs = lax.ppermute(mine, "sc", [(0, 1), (1, 0)])
    totals = jnp.where(
        core == 0,
        jnp.concatenate([mine, theirs], axis=1),
        jnp.concatenate([theirs, mine], axis=1),
    )
    pooled = (jnp.log(totals) - jnp.log(counts)[:, None]) / sharpness
    col_mean = jnp.sum(pooled, axis=0) / passages
    flops_part = jnp.sum(weights_df * col_mean * col_mean) / vocab_total
    score_part = jnp.dot(queries, pooled.T, precision=highest)
    flops_row = jnp.where(jnp.arange(passages) == 0, flops_part, 0.0)[None, :]
    summed = butterfly(
        jnp.concatenate([score_part, flops_row], axis=0), [("vy", n_vy), ("vz", n_vz)]
    )
    scores, flops_value = summed[:-1], summed[-1, 0]
    losses_each, probs = softmax_terms(scores, pairing)
    contrast = jnp.mean(losses_each)
    dscores = probs * (loss_scale / passages)
    dpooled = jnp.dot(dscores.T, queries, precision=highest) + flops_grad * weights_df * col_mean
    factor = dpooled / totals
    spread = lax.dot_general(member, factor, (((0,), (0,)), ((), ())), precision=highest)
    seventh = fourth * squared * lifted
    dlogits = jnp.where(logits > 0, spread * seventh, 0.0).astype(jnp.bfloat16)
    partial = lax.dot_general(
        full_head, dlogits, (((1,), (1,)), ((), ())), preferred_element_type=jnp.float32
    )
    grad_cols = halving_scatter(
        lax.psum_scatter(partial, "vz", scatter_dimension=0, tiled=True), "vy", n_vy
    )
    losses = jnp.stack([contrast, flops_value])
    return (grad_cols.T.astype(jnp.bfloat16), losses)


def solution(mesh):
    n_seq, n_voc = mesh.devices.shape
    n_sc = 2
    n_vy = 4
    sizes = (n_seq // n_sc, n_sc, n_voc // n_vy, n_vy)
    mesh4 = Mesh(mesh.devices.reshape(sizes), ("sx", "sc", "vz", "vy"))
    placed = (P(SEQ, None), P(SEQ, VOC), P(None, VOC), P(), P(), P(VOC))
    return jax.shard_map(
        lambda *a: per_device(sizes, *a),
        mesh=mesh4,
        in_specs=placed,
        out_specs=(P(SEQ, VOC), P()),
        check_vma=False,
    )
```

```python
import jax
import jax.numpy as jnp
from jax import lax
from jax.sharding import Mesh, PartitionSpec as P

DOCS = 4194304


sharpness = 8.0
loss_scale = 16384.0
flops_weight = 32.0
highest = lax.Precision.HIGHEST

SEQ = ("sx", "sc")
VOC = ("vz", "vy")


def rounds_of(n):
    pairs = []
    d = 1
    while 2 * d < n:
        pairs.append([(i, i ^ d) for i in range(n)])
        d *= 2
    if n > 1:
        pairs.append([(i, n - 1 - i) for i in range(n)])
    return pairs


def butterfly(x, axes_sizes):
    for ax, n in axes_sizes:
        for perm in rounds_of(n):
            x = jax.tree.map(lambda a: a + lax.ppermute(a, ax, perm), x)
    return x


def halving_scatter(x, ax, n):
    me = lax.axis_index(ax)
    d = n // 2
    while d >= 1:
        h = x.shape[0] // 2
        bit = (me // d) % 2
        keep = lax.dynamic_slice_in_dim(x, bit * h, h, 0)
        send = lax.dynamic_slice_in_dim(x, (1 - bit) * h, h, 0)
        if d == n // 2:
            perm = [(i, n - 1 - i) for i in range(n)]
        else:
            perm = [(i, i ^ d) for i in range(n)]
        x = keep + lax.ppermute(send, ax, perm)
        d //= 2
    return x


def softmax_terms(scores, pair_rows):
    onehot = (jnp.arange(scores.shape[0], dtype=jnp.int32)[:, None] == pair_rows[None, :]).astype(
        jnp.float32
    )
    peak_score = jnp.max(scores, axis=0)
    shifted = jnp.exp(scores - peak_score[None, :])
    denominator = jnp.sum(shifted, axis=0)
    log_total = peak_score + jnp.log(denominator)
    losses_each = log_total - jnp.sum(onehot * scores, axis=0)
    return (losses_each, shifted / denominator[None, :] - onehot)


def per_device(sizes, hidden, head_weight, queries, passage_lengths, pairing, doc_freq):
    n_sx, n_sc, n_vz, n_vy = sizes
    tok_rows = hidden.shape[0]
    vocab_cols = head_weight.shape[1]
    passages = passage_lengths.shape[0]
    vocab_total = vocab_cols * n_vz * n_vy
    finish = jnp.cumsum(passage_lengths)
    starts = finish - passage_lengths
    seq_index = lax.axis_index("sx") * n_sc + lax.axis_index("sc")
    position = seq_index * tok_rows + jnp.arange(tok_rows, dtype=jnp.int32)
    member = (
        (position[None, :] >= starts[:, None]) & (position[None, :] < finish[:, None])
    ).astype(jnp.float32)
    counts = passage_lengths.astype(jnp.float32)
    weights_df = jnp.log(1.0 + DOCS / (1.0 + doc_freq.astype(jnp.float32)))
    flops_grad = loss_scale * flops_weight * 2.0 / (vocab_total * passages)
    full_head = lax.all_gather(head_weight, SEQ, axis=0, tiled=True)
    logits = jnp.dot(hidden, full_head, preferred_element_type=jnp.float32)
    lifted = 1.0 + jax.nn.relu(logits)
    squared = lifted * lifted
    fourth = squared * squared
    powered = fourth * fourth
    local_sums = jnp.dot(member, powered, precision=highest)
    core = lax.axis_index("sc")
    half_cols = vocab_cols // n_sc
    own_half = lax.dynamic_slice_in_dim(local_sums, core * half_cols, half_cols, 1)
    other_half = lax.dynamic_slice_in_dim(local_sums, (1 - core) * half_cols, half_cols, 1)
    chip_half = own_half + lax.ppermute(other_half, "sc", [(0, 1), (1, 0)])
    mine = butterfly(chip_half, [("sx", n_sx)])
    theirs = lax.ppermute(mine, "sc", [(0, 1), (1, 0)])
    totals = jnp.where(
        core == 0,
        jnp.concatenate([mine, theirs], axis=1),
        jnp.concatenate([theirs, mine], axis=1),
    )
    pooled = (jnp.log(totals) - jnp.log(counts)[:, None]) / sharpness
    col_mean = jnp.sum(pooled, axis=0) / passages
    flops_part = jnp.sum(weights_df * col_mean * col_mean) / vocab_total
    score_part = jnp.dot(queries, pooled.T, precision=highest)
    flops_row = jnp.where(jnp.arange(passages) == 0, flops_part, 0.0)[None, :]
    summed = butterfly(
        jnp.concatenate([score_part, flops_row], axis=0), [("vy", n_vy), ("vz", n_vz)]
    )
    scores, flops_value = summed[:-1], summed[-1, 0]
    losses_each, probs = softmax_terms(scores, pairing)
    contrast = jnp.mean(losses_each)
    dscores = probs * (loss_scale / passages)
    dpooled = jnp.dot(dscores.T, queries, precision=highest) + flops_grad * weights_df * col_mean
    factor = dpooled / totals
    spread = lax.dot_general(member, factor, (((0,), (0,)), ((), ())), precision=highest)
    seventh = fourth * squared * lifted
    dlogits = jnp.where(logits > 0, spread * seventh, 0.0).astype(jnp.bfloat16)
    partial = lax.dot_general(
        full_head, dlogits, (((1,), (1,)), ((), ())), preferred_element_type=jnp.float32
    )
    grad_cols = halving_scatter(
        lax.psum_scatter(partial, "vz", scatter_dimension=0, tiled=True), "vy", n_vy
    )
    losses = jnp.stack([contrast, flops_value])
    return (grad_cols.T.astype(jnp.bfloat16), losses)


def solution(mesh):
    n_seq, n_voc = mesh.devices.shape
    n_sc = 2
    n_vy = 4
    sizes = (n_seq // n_sc, n_sc, n_voc // n_vy, n_vy)
    mesh4 = Mesh(mesh.devices.reshape(sizes), ("sx", "sc", "vz", "vy"))
    placed = (P(SEQ, None), P(SEQ, VOC), P(None, VOC), P(), P(), P(VOC))
    return jax.shard_map(
        lambda *a: per_device(sizes, *a),
        mesh=mesh4,
        in_specs=placed,
        out_specs=(P(SEQ, VOC), P()),
        check_vma=False,
    )
```

```python
import jax
import jax.numpy as jnp
from jax import lax
from jax.sharding import Mesh, PartitionSpec as P

DOCS = 4194304


sharpness = 8.0
loss_scale = 16384.0
flops_weight = 32.0
highest = lax.Precision.HIGHEST

SEQ = ("sx", "sc")
VOC = ("vz", "vy")


def rounds_of(n):
    if n == 8:
        second = {0: 6, 6: 0, 1: 7, 7: 1, 2: 4, 4: 2, 3: 5, 5: 3}
        return [
            [(i, i ^ 1) for i in range(n)],
            [(i, second[i]) for i in range(n)],
            [(i, i ^ 2) for i in range(n)],
        ]
    pairs = []
    d = 1
    while 2 * d < n:
        pairs.append([(i, i ^ d) for i in range(n)])
        d *= 2
    if n > 1:
        pairs.append([(i, n - 1 - i) for i in range(n)])
    return pairs


def butterfly(x, axes_sizes):
    for ax, n in axes_sizes:
        for perm in rounds_of(n):
            x = jax.tree.map(lambda a: a + lax.ppermute(a, ax, perm), x)
    return x


def halving_scatter(x, ax, n):
    me = lax.axis_index(ax)
    d = n // 2
    while d >= 1:
        h = x.shape[0] // 2
        bit = (me // d) % 2
        keep = lax.dynamic_slice_in_dim(x, bit * h, h, 0)
        send = lax.dynamic_slice_in_dim(x, (1 - bit) * h, h, 0)
        if d == n // 2:
            perm = [(i, n - 1 - i) for i in range(n)]
        else:
            perm = [(i, i ^ d) for i in range(n)]
        x = keep + lax.ppermute(send, ax, perm)
        d //= 2
    return x


def softmax_terms(scores, pair_rows):
    onehot = (jnp.arange(scores.shape[0], dtype=jnp.int32)[:, None] == pair_rows[None, :]).astype(
        jnp.float32
    )
    peak_score = jnp.max(scores, axis=0)
    shifted = jnp.exp(scores - peak_score[None, :])
    denominator = jnp.sum(shifted, axis=0)
    log_total = peak_score + jnp.log(denominator)
    losses_each = log_total - jnp.sum(onehot * scores, axis=0)
    return (losses_each, shifted / denominator[None, :] - onehot)


def per_device(sizes, hidden, head_weight, queries, passage_lengths, pairing, doc_freq):
    n_sx, n_sc, n_vz, n_vy = sizes
    tok_rows = hidden.shape[0]
    vocab_cols = head_weight.shape[1]
    passages = passage_lengths.shape[0]
    vocab_total = vocab_cols * n_vz * n_vy
    finish = jnp.cumsum(passage_lengths)
    starts = finish - passage_lengths
    seq_index = lax.axis_index("sx") * n_sc + lax.axis_index("sc")
    position = seq_index * tok_rows + jnp.arange(tok_rows, dtype=jnp.int32)
    member = (
        (position[None, :] >= starts[:, None]) & (position[None, :] < finish[:, None])
    ).astype(jnp.float32)
    counts = passage_lengths.astype(jnp.float32)
    weights_df = jnp.log(1.0 + DOCS / (1.0 + doc_freq.astype(jnp.float32)))
    flops_grad = loss_scale * flops_weight * 2.0 / (vocab_total * passages)
    full_head = lax.all_gather(head_weight, SEQ, axis=0, tiled=True)
    logits = jnp.dot(hidden, full_head, preferred_element_type=jnp.float32)
    lifted = 1.0 + jax.nn.relu(logits)
    squared = lifted * lifted
    fourth = squared * squared
    powered = fourth * fourth
    masked_seventh = lax.optimization_barrier(
        jnp.where(logits > 0, fourth * squared * lifted, 0.0)
    )
    local_sums = jnp.dot(member, powered, precision=highest)
    core = lax.axis_index("sc")
    half_cols = vocab_cols // n_sc
    own_half = lax.dynamic_slice_in_dim(local_sums, core * half_cols, half_cols, 1)
    other_half = lax.dynamic_slice_in_dim(local_sums, (1 - core) * half_cols, half_cols, 1)
    chip_half = own_half + lax.ppermute(other_half, "sc", [(0, 1), (1, 0)])
    mine = butterfly(chip_half, [("sx", n_sx)])
    theirs = lax.ppermute(mine, "sc", [(0, 1), (1, 0)])
    totals = jnp.where(
        core == 0,
        jnp.concatenate([mine, theirs], axis=1),
        jnp.concatenate([theirs, mine], axis=1),
    )
    pooled = (jnp.log(totals) - jnp.log(counts)[:, None]) / sharpness
    col_mean = jnp.sum(pooled, axis=0) / passages
    flops_part = jnp.sum(weights_df * col_mean * col_mean) / vocab_total
    score_part = jnp.dot(queries, pooled.T, precision=highest)
    flops_row = jnp.where(jnp.arange(passages) == 0, flops_part, 0.0)[None, :]
    summed = butterfly(
        jnp.concatenate([score_part, flops_row], axis=0), [("vy", n_vy), ("vz", n_vz)]
    )
    scores, flops_value = summed[:-1], summed[-1, 0]
    losses_each, probs = softmax_terms(scores, pairing)
    contrast = jnp.mean(losses_each)
    dscores = probs * (loss_scale / passages)
    dpooled = jnp.dot(dscores.T, queries, precision=highest) + flops_grad * weights_df * col_mean
    factor = dpooled / totals
    spread = lax.dot_general(member, factor, (((0,), (0,)), ((), ())), precision=highest)
    dlogits = jnp.where(masked_seventh > 0, spread * masked_seventh, 0.0).astype(jnp.bfloat16)
    partial = lax.dot_general(
        full_head, dlogits, (((1,), (1,)), ((), ())), preferred_element_type=jnp.float32
    )
    grad_cols = halving_scatter(
        lax.psum_scatter(partial, "vz", scatter_dimension=0, tiled=True), "vy", n_vy
    )
    losses = jnp.stack([contrast, flops_value])
    return (grad_cols.T.astype(jnp.bfloat16), losses)


def solution(mesh):
    n_seq, n_voc = mesh.devices.shape
    n_sc = 2
    n_vy = 4
    sizes = (n_seq // n_sc, n_sc, n_voc // n_vy, n_vy)
    mesh4 = Mesh(mesh.devices.reshape(sizes), ("sx", "sc", "vz", "vy"))
    placed = (P(SEQ, None), P(SEQ, VOC), P(None, VOC), P(), P(), P(VOC))
    return jax.shard_map(
        lambda *a: per_device(sizes, *a),
        mesh=mesh4,
        in_specs=placed,
        out_specs=(P(SEQ, VOC), P()),
        check_vma=False,
    )
```
